512 devices in a mesh: group: 8 (over x, y_hi), sub: 64 (over y_lo, z, core).
Axes of the slice: x: 4, y: 8 (y_hi: 2, y_lo: 4; y = y_hi * 4 + y_lo), z: 8, core: 2. Of those that a mesh axis runs over, the one named last changes fastest.
Arguments:
- modes: bfloat16 [524288, 512], P(('group', 'sub')), may hold values from -6 to 6
- block_vals: bfloat16 [24576, 128, 128], P(('group', 'sub')), may hold values from -0.21875 to 0.21875
- block_cols: int32 [24576], P(('group', 'sub')), may hold values from 0 to 7, as said below
- level_maps: bfloat16 [2, 128, 128], replicated, may hold values from -0.5 to 0.5
- psi: bfloat16 [524288, 512], P(('group', 'sub')), may hold values from -0.09375 to 0.09375
- parent_vals: bfloat16 [4096, 128, 128], P(('group', 'sub')), may hold values from -0.09375 to 0.09375
- parent_rows: int32 [4096], P(('group', 'sub')), may hold values from 0 to 63
Outputs:
- parent_coupling: bfloat16 [8192, 1024], P('sub', 'group')
- projected: float32 [4096, 512], P(('group', 'sub'))
The draws below stay inside these ranges and needn't reach their ends.
Inputs may be any that keep to these rules, and one draw needn't show every extreme that they name: `block_cols`: within one interface row block of one device the 6 vertex blocks are distinct.
All inputs are finite; a program needn't handle non-finite values.
Results may differ from the reference program's by a relative error of at most 0.0078.
Values may be sent and summed in bfloat16 or wider, within the bound.
No kernel may reach another device: no remote copies, remote signals or barrier semaphores. Data moves between devices by JAX's collectives and lax.ppermute only.
A program may use at most 64 MiB of HBM per device.

```python
import jax
import jax.numpy as jnp
import numpy as np
from jax import lax

MODES = 512
BLK = 128
ROWS_DEV = 1024
IFB = 8
BPR = 6
NPB = 8
IF_DEV = 1024
NCB = 8
LEVELS = 2
MERGED = 4
BLOCK_ROWS = 4096
N_GROUP = 8
N_SUB = 64


def draw_block_cols(key, part):
    subkeys = jax.random.split(jax.random.fold_in(key, 11), BLOCK_ROWS)
    chosen = jax.vmap(lambda subkey: jax.random.permutation(subkey, NCB)[:BPR])(subkeys)
    return chosen.reshape(-1).astype(jnp.int32)


def plant(values, own_key, least, high):
    dims = values.shape
    index_at = [jax.random.randint(jax.random.fold_in(own_key, axis), (), 0, dims[axis]) for axis in range(len(dims))]
    values = values.at[tuple(index_at)].set(least)
    longest = dims.index(max(dims))
    index_at[longest] = (index_at[longest] + 1) % dims[longest]
    return values.at[tuple(index_at)].set(high)


def strengthened(array, rng, source, target, shards_of, factor):
    def block_of(position):
        return (jnp.arange(array.shape[position]) // (array.shape[position] // shards_of)).reshape((-1,) + (1,) * (array.ndim - 1 - position))

    near = jax.random.permutation(rng, shards_of)[block_of(target)]
    second = (block_of(target) + shards_of // 2) % shards_of
    return jnp.where((block_of(source) == near) | (block_of(source) == second), factor * array, array)


def levels(own_key, shape, shards, smallest, top_value):
    level = 1.0
    for position, parts in shards:
        steps = jax.random.uniform(jax.random.fold_in(jax.random.fold_in(own_key, 6), position), (parts,), jnp.float32, smallest / len(shards), top_value / len(shards))
        level = level * jnp.repeat(jnp.exp(steps), shape[position] // parts).reshape((-1,) + (1,) * (len(shape) - 1 - position))
    return level


def normal_values(rng, dims, scale, limit, cuts=(), kind=jnp.bfloat16):
    drawn = scale * jax.random.normal(rng, dims, jnp.float32)
    if cuts:
        drawn = drawn * levels(rng, dims, cuts, -0.22, 0.18)
    return jnp.clip(drawn, -limit, limit).astype(kind)


def heavy_noise(own_key, dims, width, limit, shards, heavy, dtype=jnp.bfloat16):
    values = width * jax.random.normal(own_key, dims, jnp.float32)
    if shards:
        values = values * levels(own_key, dims, shards, -0.22, 0.18)
    return jnp.clip(strengthened(values, jax.random.fold_in(own_key, 3), *heavy), -limit, limit).astype(dtype)


def setup_inputs(seed: int = 0) -> dict:
    streams_of = jax.random.split(jax.random.key(seed), 8)
    modes = normal_values(streams_of[0], (N_GROUP * N_SUB * ROWS_DEV, MODES), 1.0, 6.0, ((0, 512),))
    block_vals = normal_values(streams_of[1], (BLOCK_ROWS * BPR, BLK, BLK), (BPR * BLK) ** -0.5, 0.21875, ((0, 512),))
    block_cols = draw_block_cols(jax.random.fold_in(streams_of[7], 71), 0)
    level_maps = normal_values(streams_of[3], (LEVELS, BLK, BLK), BLK ** -0.5, 0.5)
    psi = heavy_noise(streams_of[4], (N_GROUP * N_SUB * IF_DEV, MODES), (N_SUB * IF_DEV) ** -0.5, 0.09375, ((0, 512),), (0, 1, 512, 6.0))
    parent_vals = normal_values(streams_of[5], (N_GROUP * N_SUB * NPB, BLK, BLK), (BLK * NPB * MERGED) ** -0.5, 0.09375, ((0, 512),))
    parent_rows = plant(jax.random.randint(streams_of[6], (N_GROUP * N_SUB * NPB,), 0, N_SUB), jax.random.fold_in(streams_of[6], 1), 0, N_SUB - 1).astype(jnp.int32)
    return dict(modes=modes, block_vals=block_vals, block_cols=block_cols, level_maps=level_maps, psi=psi, parent_vals=parent_vals, parent_rows=parent_rows)


def assemble(cols_dev, vals_dev):
    onehot = (cols_dev.reshape(IFB, BPR)[:, :, None] == jnp.arange(NCB)[None, None, :]).astype(jnp.float32)
    blocks = vals_dev.astype(jnp.float32).reshape(IFB, BPR, BLK, BLK)
    dense = jnp.einsum('rbc,rbij->ricj', onehot, blocks).reshape(IF_DEV, NCB * BLK)
    return dense.astype(jnp.bfloat16)


def coupling(inputs):
    modes_dev, vals_dev, cols_dev = inputs
    dense = assemble(cols_dev, vals_dev)
    return jnp.dot(dense, modes_dev, preferred_element_type=jnp.float32).astype(jnp.bfloat16)


def reference(modes, block_vals, block_cols, level_maps, psi, parent_vals, parent_rows):
    count = N_GROUP * N_SUB
    panels = lax.map(coupling, (modes.reshape(count, ROWS_DEV, MODES), block_vals.reshape(count, IFB * BPR, BLK, BLK), block_cols.reshape(count, IFB * BPR)))
    panels = panels.reshape(N_GROUP, N_SUB, IF_DEV, MODES)
    for level in range(LEVELS):
        partner = np.arange(N_GROUP) ^ (1 << level)
        transform = level_maps[level].astype(jnp.float32)

        def merge_level(pair):
            total = (pair[0].astype(jnp.float32) + pair[1].astype(jnp.float32)).astype(jnp.bfloat16)
            blocks = total.astype(jnp.float32).reshape(N_SUB, IFB, BLK, MODES)
            mapped = jnp.einsum('ab,srbm->sram', transform, blocks)
            return mapped.reshape(N_SUB, IF_DEV, MODES).astype(jnp.bfloat16)

        panels = lax.map(merge_level, (panels, panels[partner]))
    heads = panels[:, :, :BLK, :]
    rows_all = parent_rows.reshape(N_GROUP, N_SUB, NPB)
    vals_all = parent_vals.reshape(N_GROUP, N_SUB, NPB, BLK, BLK)

    def group_terms(inputs):
        head_group, rows_group, vals_group = inputs
        picked = head_group[rows_group]
        return jnp.einsum('skab,skbm->sam', vals_group.astype(jnp.float32), picked.astype(jnp.float32))

    terms = lax.map(group_terms, (heads, rows_all, vals_all))
    summed = terms.reshape(N_GROUP // MERGED, MERGED, N_SUB, BLK, MODES).sum(axis=1).astype(jnp.bfloat16)
    parent_coupling = summed.transpose(1, 2, 0, 3).reshape(N_SUB * BLK, (N_GROUP // MERGED) * MODES)

    def group_projection(inputs):
        psi_group, panel_group = inputs
        return jnp.einsum('sim,sin->mn', psi_group.astype(jnp.float32), panel_group.astype(jnp.float32))

    projected = lax.map(group_projection, (psi.reshape(N_GROUP, N_SUB, IF_DEV, MODES), panels))
    return parent_coupling, projected.reshape(N_GROUP * MODES, MODES)
```

```python
import jax
import jax.numpy as jnp
from jax import lax
from jax.sharding import PartitionSpec as P

IFB = 8
BPR = 6


def from_partner(value, axis, mask):
    pairs = [(source, source ^ mask) for source in range(lax.axis_size(axis))]
    return lax.ppermute(value, axis, pairs)


def on_device(modes, block_vals, block_cols, level_maps, psi, parent_vals, parent_rows):
    block_size = block_vals.shape[1]
    width = modes.shape[1]
    vertex_blocks = modes.shape[0] // block_size
    row_blocks = IFB
    levels = min(2, lax.axis_size("group").bit_length() - 1)
    merged = 2**levels
    n_sub = lax.axis_size("sub")
    group_index = lax.axis_index("group")

    vals_all = [parent_vals]
    rows_all = [parent_rows]
    for mask in range(1, merged):
        vals_all.append(from_partner(parent_vals, "group", mask))
        rows_all.append(from_partner(parent_rows, "group", mask))
    vals_all = jnp.concatenate(vals_all, axis=0)
    rows_all = jnp.concatenate(rows_all, axis=0)

    onehot = (
        block_cols.reshape(row_blocks, BPR)[:, :, None] == jnp.arange(vertex_blocks)[None, None, :]
    ).astype(jnp.float32)
    blocks = block_vals.astype(jnp.float32).reshape(row_blocks, BPR, block_size, block_size)
    dense = (
        jnp.einsum("rbc,rbij->ricj", onehot, blocks)
        .reshape(row_blocks * block_size, vertex_blocks * block_size)
        .astype(jnp.bfloat16)
    )
    panel = jnp.dot(dense, modes, preferred_element_type=jnp.float32).astype(jnp.bfloat16)
    for level in range(levels):
        sibling = from_partner(panel, "group", 2**level)
        total = (panel.astype(jnp.float32) + sibling.astype(jnp.float32)).astype(jnp.bfloat16)
        mapped = jnp.einsum(
            "ab,rbm->ram",
            level_maps[level],
            total.reshape(row_blocks, block_size, width),
            preferred_element_type=jnp.float32,
        )
        panel = mapped.reshape(row_blocks * block_size, width).astype(jnp.bfloat16)

    quarter = width // merged
    column = (group_index % merged) * quarter
    head = lax.dynamic_slice_in_dim(panel[:block_size], column, quarter, 1)
    piece = lax.all_gather(head, "sub", axis=0, tiled=True).reshape(n_sub, block_size, quarter)
    picked = jnp.take(piece, rows_all, axis=0)
    parent_out = jnp.einsum(
        "kab,kbm->am", vals_all, picked, preferred_element_type=jnp.float32
    ).astype(jnp.bfloat16)

    partial = lax.dot_general(psi, panel, (((0,), (0,)), ((), ())), preferred_element_type=jnp.float32)
    spread = lax.all_to_all(partial.reshape(n_sub, width // n_sub, width), "sub", 0, 0, tiled=True)
    projected = spread.sum(axis=0)
    return (parent_out, projected)


def solution(mesh):
    return jax.shard_map(
        on_device,
        mesh=mesh,
        in_specs=(
            P(("group", "sub"), None),
            P(("group", "sub"), None, None),
            P(("group", "sub")),
            P(),
            P(("group", "sub"), None),
            P(("group", "sub"), None, None),
            P(("group", "sub")),
        ),
        out_specs=(P("sub", "group"), P(("group", "sub"), None)),
        check_vma=False,
    )
```

```python
import jax
import jax.numpy as jnp
from jax import lax
from jax.sharding import PartitionSpec as P

IFB = 8
BPR = 6


def from_partner(value, axis, mask):
    pairs = [(source, source ^ mask) for source in range(lax.axis_size(axis))]
    return lax.ppermute(value, axis, pairs)


def on_device(modes, block_vals, block_cols, level_maps, psi, parent_vals, parent_rows):
    block_size = block_vals.shape[1]
    width = modes.shape[1]
    vertex_blocks = modes.shape[0] // block_size
    row_blocks = IFB
    levels = min(2, lax.axis_size("group").bit_length() - 1)
    merged = 2**levels
    n_sub = lax.axis_size("sub")
    n_parent = parent_vals.shape[0]
    group_index = lax.axis_index("group")
    core = lax.axis_index("sub") % 2

    rows_as_block = jnp.zeros((16, block_size), jnp.bfloat16).at[0, :n_parent].set(parent_rows.astype(jnp.bfloat16))
    packed = jnp.concatenate([parent_vals.reshape(n_parent * block_size, block_size), rows_as_block], axis=0)
    packs = [packed] + [from_partner(packed, "group", mask) for mask in range(1, merged)]
    vals_all = jnp.concatenate([p[: n_parent * block_size] for p in packs], axis=0).reshape(-1, block_size, block_size)
    rows_all = jnp.concatenate([p[n_parent * block_size, :n_parent] for p in packs]).astype(jnp.int32)

    onehot = (
        block_cols.reshape(row_blocks, BPR)[:, :, None] == jnp.arange(vertex_blocks)[None, None, :]
    ).astype(jnp.float32)
    blocks = block_vals.astype(jnp.float32).reshape(row_blocks, BPR, block_size, block_size)
    dense = (
        jnp.einsum("rbc,rbij->ricj", onehot, blocks)
        .reshape(row_blocks * block_size, vertex_blocks * block_size)
        .astype(jnp.bfloat16)
    )
    panel = jnp.dot(dense, modes, preferred_element_type=jnp.float32).astype(jnp.bfloat16)
    for level in range(levels):
        sibling = from_partner(panel, "group", 2**level)
        total = (panel.astype(jnp.float32) + sibling.astype(jnp.float32)).astype(jnp.bfloat16)
        mapped = jnp.einsum(
            "ab,rbm->ram",
            level_maps[level],
            total.reshape(row_blocks, block_size, width),
            preferred_element_type=jnp.float32,
        )
        panel = mapped.reshape(row_blocks * block_size, width).astype(jnp.bfloat16)

    quarter = width // merged
    half_rows = block_size // 2
    column = (group_index % merged) * quarter
    head = lax.dynamic_slice_in_dim(panel[:block_size], column, quarter, 1)
    outgoing = jnp.tile(head.reshape(2, half_rows, quarter), (n_sub // 2, 1, 1))
    mine = lax.all_to_all(outgoing, "sub", 0, 0, tiled=True)
    theirs = from_partner(mine, "sub", 1)
    picked_mine = jnp.take(mine, rows_all, axis=0)
    picked_theirs = jnp.take(theirs, rows_all, axis=0)
    picked_low = jnp.where(core == 0, picked_mine, picked_theirs)
    picked_high = jnp.where(core == 0, picked_theirs, picked_mine)
    parent_sum = jnp.einsum(
        "kab,kbm->am", vals_all[:, :, :half_rows], picked_low, preferred_element_type=jnp.float32
    ) + jnp.einsum("kab,kbm->am", vals_all[:, :, half_rows:], picked_high, preferred_element_type=jnp.float32)
    parent_out = parent_sum.astype(jnp.bfloat16)

    half = width // 2
    keep_cols = lax.dynamic_slice_in_dim(panel, core * half, half, 1)
    send_cols = lax.dynamic_slice_in_dim(panel, (1 - core) * half, half, 1)
    contract = (((0,), (0,)), ((), ()))
    keep = lax.dot_general(psi, keep_cols, contract, preferred_element_type=jnp.float32)
    send = lax.dot_general(psi, send_cols, contract, preferred_element_type=jnp.float32)
    chip_sum = keep + from_partner(send, "sub", 1)
    spread = lax.all_to_all(chip_sum.reshape(n_sub, width // n_sub, half), "sub", 0, 0, tiled=True)
    by_half = spread.reshape(n_sub // 2, 2, width // n_sub, half).sum(axis=0)
    projected = by_half.transpose(1, 0, 2).reshape(width // n_sub, width)
    return (parent_out, projected)


def solution(mesh):
    return jax.shard_map(
        on_device,
        mesh=mesh,
        in_specs=(
            P(("group", "sub"), None),
            P(("group", "sub"), None, None),
            P(("group", "sub")),
            P(),
            P(("group", "sub"), None),
            P(("group", "sub"), None, None),
            P(("group", "sub")),
        ),
        out_specs=(P("sub", "group"), P(("group", "sub"), None)),
        check_vma=False,
    )
```

```python
import jax
import jax.numpy as jnp
from jax import lax
from jax.sharding import PartitionSpec as P

IFB = 8
BPR = 6


def from_partner(value, axis, mask):
    pairs = [(source, source ^ mask) for source in range(lax.axis_size(axis))]
    return lax.ppermute(value, axis, pairs)


def on_device(modes, block_vals, block_cols, level_maps, psi, parent_vals, parent_rows):
    block_size = block_vals.shape[1]
    width = modes.shape[1]
    vertex_blocks = modes.shape[0] // block_size
    row_blocks = IFB
    levels = min(2, lax.axis_size("group").bit_length() - 1)
    merged = 2**levels
    n_sub = lax.axis_size("sub")
    n_parent = parent_vals.shape[0]
    group_index = lax.axis_index("group")
    core = lax.axis_index("sub") % 2

    rows_as_block = jnp.zeros((16, block_size), jnp.bfloat16).at[0, :n_parent].set(parent_rows.astype(jnp.bfloat16))
    packed = jnp.concatenate([parent_vals.reshape(n_parent * block_size, block_size), rows_as_block], axis=0)
    packs = [packed] + [from_partner(packed, "group", mask) for mask in range(1, merged)]
    vals_all = jnp.concatenate([p[: n_parent * block_size] for p in packs], axis=0).reshape(-1, block_size, block_size)
    rows_all = jnp.concatenate([p[n_parent * block_size, :n_parent] for p in packs]).astype(jnp.int32)

    onehot = (
        block_cols.reshape(row_blocks, BPR)[:, :, None] == jnp.arange(vertex_blocks)[None, None, :]
    ).astype(jnp.float32)
    blocks = block_vals.astype(jnp.float32).reshape(row_blocks, BPR, block_size, block_size)
    dense = (
        jnp.einsum("rbc,rbij->ricj", onehot, blocks)
        .reshape(row_blocks * block_size, vertex_blocks * block_size)
        .astype(jnp.bfloat16)
    )
    panel = jnp.dot(dense, modes, preferred_element_type=jnp.float32).astype(jnp.bfloat16)

    held = panel
    for level in reversed(range(levels)):
        half_len = held.shape[0] // 2
        upper = (group_index >> level) & 1
        keep = lax.dynamic_slice_in_dim(held, upper * half_len, half_len, 0)
        away = lax.dynamic_slice_in_dim(held, (1 - upper) * half_len, half_len, 0)
        total = keep.astype(jnp.float32) + from_partner(away, "group", 2**level).astype(jnp.float32)
        held = total if level == 0 else total.astype(jnp.bfloat16)
    mapped = held.reshape(-1, block_size, width)
    for level in range(levels):
        mapped = jnp.einsum(
            "ab,rbm->ram", level_maps[level].astype(jnp.float32), mapped, preferred_element_type=jnp.float32
        )
    piece = mapped.reshape(-1, width).astype(jnp.bfloat16)
    vals_all, rows_all, piece = lax.optimization_barrier((vals_all, rows_all, piece))
    for level in range(levels):
        upper = (group_index >> level) & 1
        other = from_partner(piece, "group", 2**level)
        piece = jnp.where(upper == 0, jnp.concatenate([piece, other], 0), jnp.concatenate([other, piece], 0))
    panel = piece

    quarter = width // merged
    half_rows = block_size // 2
    column = (group_index % merged) * quarter
    head = lax.dynamic_slice_in_dim(panel[:block_size], column, quarter, 1)
    outgoing = jnp.tile(head.reshape(2, half_rows, quarter), (n_sub // 2, 1, 1))
    mine = lax.all_to_all(outgoing, "sub", 0, 0, tiled=True)
    theirs = from_partner(mine, "sub", 1)
    picked_mine = jnp.take(mine, rows_all, axis=0)
    picked_theirs = jnp.take(theirs, rows_all, axis=0)
    picked_low = jnp.where(core == 0, picked_mine, picked_theirs)
    picked_high = jnp.where(core == 0, picked_theirs, picked_mine)
    parent_sum = jnp.einsum(
        "kab,kbm->am", vals_all[:, :, :half_rows], picked_low, preferred_element_type=jnp.float32
    ) + jnp.einsum("kab,kbm->am", vals_all[:, :, half_rows:], picked_high, preferred_element_type=jnp.float32)
    parent_out = parent_sum.astype(jnp.bfloat16)

    half = width // 2
    keep_cols = lax.dynamic_slice_in_dim(panel, core * half, half, 1)
    send_cols = lax.dynamic_slice_in_dim(panel, (1 - core) * half, half, 1)
    contract = (((0,), (0,)), ((), ()))
    keep = lax.dot_general(psi, keep_cols, contract, preferred_element_type=jnp.float32)
    send = lax.dot_general(psi, send_cols, contract, preferred_element_type=jnp.float32)
    chip_sum = keep + from_partner(send, "sub", 1)
    spread = lax.all_to_all(chip_sum.reshape(n_sub, width // n_sub, half), "sub", 0, 0, tiled=True)
    by_half = spread.reshape(n_sub // 2, 2, width // n_sub, half).sum(axis=0)
    projected = by_half.transpose(1, 0, 2).reshape(width // n_sub, width)
    return (parent_out, projected)


def solution(mesh):
    return jax.shard_map(
        on_device,
        mesh=mesh,
        in_specs=(
            P(("group", "sub"), None),
            P(("group", "sub"), None, None),
            P(("group", "sub")),
            P(),
            P(("group", "sub"), None),
            P(("group", "sub"), None, None),
            P(("group", "sub")),
        ),
        out_specs=(P("sub", "group"), P(("group", "sub"), None)),
        check_vma=False,
    )
```

```python
import jax
import jax.numpy as jnp
from jax import lax
from jax.sharding import PartitionSpec as P

IFB = 8
BPR = 6


def from_partner(value, axis, mask):
    pairs = [(source, source ^ mask) for source in range(lax.axis_size(axis))]
    return lax.ppermute(value, axis, pairs)


def on_device(modes, block_vals, block_cols, level_maps, psi, parent_vals, parent_rows):
    block_size = block_vals.shape[1]
    width = modes.shape[1]
    vertex_blocks = modes.shape[0] // block_size
    row_blocks = IFB
    levels = min(2, lax.axis_size("group").bit_length() - 1)
    merged = 2**levels
    n_sub = lax.axis_size("sub")
    n_parent = parent_vals.shape[0]
    group_index = lax.axis_index("group")
    core = lax.axis_index("sub") % 2

    rows_as_block = jnp.zeros((16, block_size), jnp.bfloat16).at[0, :n_parent].set(parent_rows.astype(jnp.bfloat16))
    packed = jnp.concatenate([parent_vals.reshape(n_parent * block_size, block_size), rows_as_block], axis=0)

    onehot = (
        block_cols.reshape(row_blocks, BPR)[:, :, None] == jnp.arange(vertex_blocks)[None, None, :]
    ).astype(jnp.float32)
    blocks = block_vals.astype(jnp.float32).reshape(row_blocks, BPR, block_size, block_size)
    dense = (
        jnp.einsum("rbc,rbij->ricj", onehot, blocks)
        .reshape(row_blocks * block_size, vertex_blocks * block_size)
        .astype(jnp.bfloat16)
    )
    panel = jnp.dot(dense, modes, preferred_element_type=jnp.float32).astype(jnp.bfloat16)
    carried = packed[None]
    for level in range(levels):
        sibling = from_partner(panel, "group", 2**level)
        partner = levels - 1 - level
        carried, panel = lax.optimization_barrier((carried, panel))
        arrived = from_partner(carried, "group", 2**partner)
        total = (panel.astype(jnp.float32) + sibling.astype(jnp.float32)).astype(jnp.bfloat16)
        if level < levels - 1:
            arrived, total = lax.optimization_barrier((arrived, total))
        carried = jnp.concatenate([carried, arrived], axis=0)
        mapped = jnp.einsum(
            "ab,rbm->ram",
            level_maps[level],
            total.reshape(row_blocks, block_size, width),
            preferred_element_type=jnp.float32,
        )
        panel = mapped.reshape(row_blocks * block_size, width).astype(jnp.bfloat16)
    vals_all = carried[:, : n_parent * block_size].reshape(-1, block_size, block_size)
    rows_all = carried[:, n_parent * block_size, :n_parent].reshape(-1).astype(jnp.int32)

    quarter = width // merged
    half_rows = block_size // 2
    column = (group_index % merged) * quarter
    head = lax.dynamic_slice_in_dim(panel[:block_size], column, quarter, 1)
    outgoing = jnp.tile(head.reshape(2, half_rows, quarter), (n_sub // 2, 1, 1))
    mine = lax.all_to_all(outgoing, "sub", 0, 0, tiled=True)
    theirs = from_partner(mine, "sub", 1)
    picked_mine = jnp.take(mine, rows_all, axis=0)
    picked_theirs = jnp.take(theirs, rows_all, axis=0)
    picked_low = jnp.where(core == 0, picked_mine, picked_theirs)
    picked_high = jnp.where(core == 0, picked_theirs, picked_mine)
    parent_sum = jnp.einsum(
        "kab,kbm->am", vals_all[:, :, :half_rows], picked_low, preferred_element_type=jnp.float32
    ) + jnp.einsum("kab,kbm->am", vals_all[:, :, half_rows:], picked_high, preferred_element_type=jnp.float32)
    parent_out = parent_sum.astype(jnp.bfloat16)

    half = width // 2
    keep_cols = lax.dynamic_slice_in_dim(panel, core * half, half, 1)
    send_cols = lax.dynamic_slice_in_dim(panel, (1 - core) * half, half, 1)
    contract = (((0,), (0,)), ((), ()))
    keep = lax.dot_general(psi, keep_cols, contract, preferred_element_type=jnp.float32)
    send = lax.dot_general(psi, send_cols, contract, preferred_element_type=jnp.float32)
    chip_sum = keep + from_partner(send, "sub", 1)
    spread = lax.all_to_all(chip_sum.reshape(n_sub, width // n_sub, half), "sub", 0, 0, tiled=True)
    by_half = spread.reshape(n_sub // 2, 2, width // n_sub, half).sum(axis=0)
    projected = by_half.transpose(1, 0, 2).reshape(width // n_sub, width)
    return (parent_out, projected)


def solution(mesh):
    return jax.shard_map(
        on_device,
        mesh=mesh,
        in_specs=(
            P(("group", "sub"), None),
            P(("group", "sub"), None, None),
            P(("group", "sub")),
            P(),
            P(("group", "sub"), None),
            P(("group", "sub"), None, None),
            P(("group", "sub")),
        ),
        out_specs=(P("sub", "group"), P(("group", "sub"), None)),
        check_vma=False,
    )
```

```python
import jax
import jax.numpy as jnp
from jax import lax
from jax.sharding import PartitionSpec as P

IFB = 8
BPR = 6


def from_partner(value, axis, mask):
    pairs = [(source, source ^ mask) for source in range(lax.axis_size(axis))]
    return lax.ppermute(value, axis, pairs)


def on_device(modes, block_vals, block_cols, level_maps, psi, parent_vals, parent_rows):
    block_size = block_vals.shape[1]
    width = modes.shape[1]
    vertex_blocks = modes.shape[0] // block_size
    row_blocks = IFB
    levels = min(2, lax.axis_size("group").bit_length() - 1)
    merged = 2**levels
    n_sub = lax.axis_size("sub")
    n_parent = parent_vals.shape[0]
    group_index = lax.axis_index("group")
    core = lax.axis_index("sub") % 2

    rows_as_block = jnp.zeros((16, block_size), jnp.bfloat16).at[0, :n_parent].set(parent_rows.astype(jnp.bfloat16))
    packed = jnp.concatenate([parent_vals.reshape(n_parent * block_size, block_size), rows_as_block], axis=0)

    onehot = (
        block_cols.reshape(row_blocks, BPR)[:, :, None] == jnp.arange(vertex_blocks)[None, None, :]
    ).astype(jnp.float32)
    blocks = block_vals.astype(jnp.float32).reshape(row_blocks, BPR, block_size, block_size)
    dense = (
        jnp.einsum("rbc,rbij->ricj", onehot, blocks)
        .reshape(row_blocks * block_size, vertex_blocks * block_size)
        .astype(jnp.bfloat16)
    )
    panel = jnp.dot(dense, modes, preferred_element_type=jnp.float32).astype(jnp.bfloat16)
    carried = packed[None]
    for level in range(levels):
        sibling = from_partner(panel, "group", 2**level)
        partner = levels - 1 - level
        carried, panel = lax.optimization_barrier((carried, panel))
        arrived = from_partner(carried, "group", 2**partner)
        total = (panel.astype(jnp.float32) + sibling.astype(jnp.float32)).astype(jnp.bfloat16)
        if level < levels - 1:
            arrived, total = lax.optimization_barrier((arrived, total))
        carried = jnp.concatenate([carried, arrived], axis=0)
        mapped = jnp.einsum(
            "ab,rbm->ram",
            level_maps[level],
            total.reshape(row_blocks, block_size, width),
            preferred_element_type=jnp.float32,
        )
        panel = mapped.reshape(row_blocks * block_size, width).astype(jnp.bfloat16)
    quarter = width // merged
    half_rows = block_size // 2
    column = (group_index % merged) * quarter
    head = lax.dynamic_slice_in_dim(panel[:block_size], column, quarter, 1)
    carried, head = lax.optimization_barrier((carried, head))
    vals_all = carried[:, : n_parent * block_size].reshape(-1, block_size, block_size)
    rows_all = carried[:, n_parent * block_size, :n_parent].reshape(-1).astype(jnp.int32)
    outgoing = jnp.tile(head.reshape(2, half_rows, quarter), (n_sub // 2, 1, 1))
    mine = lax.all_to_all(outgoing, "sub", 0, 0, tiled=True)
    theirs = from_partner(mine, "sub", 1)
    picked_mine = jnp.take(mine, rows_all, axis=0)
    picked_theirs = jnp.take(theirs, rows_all, axis=0)
    picked_low = jnp.where(core == 0, picked_mine, picked_theirs)
    picked_high = jnp.where(core == 0, picked_theirs, picked_mine)
    parent_sum = jnp.einsum(
        "kab,kbm->am", vals_all[:, :, :half_rows], picked_low, preferred_element_type=jnp.float32
    ) + jnp.einsum("kab,kbm->am", vals_all[:, :, half_rows:], picked_high, preferred_element_type=jnp.float32)
    parent_out = parent_sum.astype(jnp.bfloat16)

    half = width // 2
    keep_cols = lax.dynamic_slice_in_dim(panel, core * half, half, 1)
    send_cols = lax.dynamic_slice_in_dim(panel, (1 - core) * half, half, 1)
    contract = (((0,), (0,)), ((), ()))
    keep = lax.dot_general(psi, keep_cols, contract, preferred_element_type=jnp.float32)
    send = lax.dot_general(psi, send_cols, contract, preferred_element_type=jnp.float32)
    chip_sum = keep + from_partner(send, "sub", 1)
    spread = lax.all_to_all(chip_sum.reshape(n_sub, width // n_sub, half), "sub", 0, 0, tiled=True)
    by_half = spread.reshape(n_sub // 2, 2, width // n_sub, half).sum(axis=0)
    projected = by_half.transpose(1, 0, 2).reshape(width // n_sub, width)
    return (parent_out, projected)


def solution(mesh):
    return jax.shard_map(
        on_device,
        mesh=mesh,
        in_specs=(
            P(("group", "sub"), None),
            P(("group", "sub"), None, None),
            P(("group", "sub")),
            P(),
            P(("group", "sub"), None),
            P(("group", "sub"), None, None),
            P(("group", "sub")),
        ),
        out_specs=(P("sub", "group"), P(("group", "sub"), None)),
        check_vma=False,
    )
```

```python
import jax
import jax.numpy as jnp
from jax import lax
from jax.sharding import PartitionSpec as P

IFB = 8
BPR = 6


def from_partner(value, axis, mask):
    pairs = [(source, source ^ mask) for source in range(lax.axis_size(axis))]
    return lax.ppermute(value, axis, pairs)


def on_device(modes, block_vals, block_cols, level_maps, psi, parent_vals, parent_rows):
    block_size = block_vals.shape[1]
    width = modes.shape[1]
    vertex_blocks = modes.shape[0] // block_size
    row_blocks = IFB
    levels = min(2, lax.axis_size("group").bit_length() - 1)
    merged = 2**levels
    n_sub = lax.axis_size("sub")
    n_parent = parent_vals.shape[0]
    group_index = lax.axis_index("group")
    core = lax.axis_index("sub") % 2

    rows_as_block = jnp.zeros((16, block_size), jnp.bfloat16).at[0, :n_parent].set(parent_rows.astype(jnp.bfloat16))
    packed = jnp.concatenate([parent_vals.reshape(n_parent * block_size, block_size), rows_as_block], axis=0)

    onehot = (
        block_cols.reshape(row_blocks, BPR)[:, :, None] == jnp.arange(vertex_blocks)[None, None, :]
    ).astype(jnp.float32)
    blocks = block_vals.astype(jnp.float32).reshape(row_blocks, BPR, block_size, block_size)
    dense = (
        jnp.einsum("rbc,rbij->ricj", onehot, blocks)
        .reshape(row_blocks * block_size, vertex_blocks * block_size)
        .astype(jnp.bfloat16)
    )
    panel = jnp.dot(dense, modes, preferred_element_type=jnp.float32).astype(jnp.bfloat16)
    carried = packed[None]
    for level in range(levels):
        sibling = from_partner(panel, "group", 2**level)
        partner = levels - 1 - level
        carried, panel = lax.optimization_barrier((carried, panel))
        arrived = from_partner(carried, "group", 2**partner)
        total = (panel.astype(jnp.float32) + sibling.astype(jnp.float32)).astype(jnp.bfloat16)
        if level < levels - 1:
            arrived, total = lax.optimization_barrier((arrived, total))
        carried = jnp.concatenate([carried, arrived], axis=0)
        mapped = jnp.einsum(
            "ab,rbm->ram",
            level_maps[level],
            total.reshape(row_blocks, block_size, width),
            preferred_element_type=jnp.float32,
        )
        panel = mapped.reshape(row_blocks * block_size, width).astype(jnp.bfloat16)
    quarter = width // merged
    half_rows = block_size // 2
    column = (group_index % merged) * quarter
    head = lax.dynamic_slice_in_dim(panel[:block_size], column, quarter, 1)
    carried, head = lax.optimization_barrier((carried, head))
    vals_all = carried[:, : n_parent * block_size].reshape(-1, block_size, block_size)
    rows_all = carried[:, n_parent * block_size, :n_parent].reshape(-1).astype(jnp.int32)
    outgoing = jnp.tile(head.reshape(2, half_rows, quarter), (n_sub // 2, 1, 1))

    half = width // 2
    keep_cols = lax.dynamic_slice_in_dim(panel, core * half, half, 1)
    send_cols = lax.dynamic_slice_in_dim(panel, (1 - core) * half, half, 1)
    contract = (((0,), (0,)), ((), ()))
    keep = lax.dot_general(psi, keep_cols, contract, preferred_element_type=jnp.float32)
    send = lax.dot_general(psi, send_cols, contract, preferred_element_type=jnp.float32)
    chip_sum = (keep + from_partner(send, "sub", 1)).reshape(n_sub, width // n_sub, half)
    high = lax.reduce_precision(chip_sum, exponent_bits=8, mantissa_bits=7)
    low = chip_sum - high
    split = jnp.stack([high.astype(jnp.bfloat16), low.astype(jnp.bfloat16)], axis=1).reshape(n_sub, -1, quarter)
    outgoing = jnp.concatenate([outgoing, split], axis=1)
    arrived = lax.all_to_all(outgoing, "sub", 0, 0, tiled=True)
    mine = arrived[:, :half_rows]
    parts = arrived[:, half_rows:].reshape(n_sub, 2, width // n_sub, half).astype(jnp.float32)
    spread = parts[:, 0] + parts[:, 1]
    by_half = spread.reshape(n_sub // 2, 2, width // n_sub, half).sum(axis=0)
    projected = by_half.transpose(1, 0, 2).reshape(width // n_sub, width)

    theirs = from_partner(mine, "sub", 1)
    picked_mine = jnp.take(mine, rows_all, axis=0)
    picked_theirs = jnp.take(theirs, rows_all, axis=0)
    picked_low = jnp.where(core == 0, picked_mine, picked_theirs)
    picked_high = jnp.where(core == 0, picked_theirs, picked_mine)
    parent_sum = jnp.einsum(
        "kab,kbm->am", vals_all[:, :, :half_rows], picked_low, preferred_element_type=jnp.float32
    ) + jnp.einsum("kab,kbm->am", vals_all[:, :, half_rows:], picked_high, preferred_element_type=jnp.float32)
    parent_out = parent_sum.astype(jnp.bfloat16)
    return (parent_out, projected)


def solution(mesh):
    return jax.shard_map(
        on_device,
        mesh=mesh,
        in_specs=(
            P(("group", "sub"), None),
            P(("group", "sub"), None, None),
            P(("group", "sub")),
            P(),
            P(("group", "sub"), None),
            P(("group", "sub"), None, None),
            P(("group", "sub")),
        ),
        out_specs=(P("sub", "group"), P(("group", "sub"), None)),
        check_vma=False,
    )
```

```python
import jax
import jax.numpy as jnp
from jax import lax
from jax.sharding import PartitionSpec as P

IFB = 8
BPR = 6


def from_partner(value, axis, mask):
    pairs = [(source, source ^ mask) for source in range(lax.axis_size(axis))]
    return lax.ppermute(value, axis, pairs)


def on_device(modes, block_vals, block_cols, level_maps, psi, parent_vals, parent_rows):
    block_size = block_vals.shape[1]
    width = modes.shape[1]
    vertex_blocks = modes.shape[0] // block_size
    row_blocks = IFB
    levels = min(2, lax.axis_size("group").bit_length() - 1)
    merged = 2**levels
    n_sub = lax.axis_size("sub")
    n_parent = parent_vals.shape[0]
    group_index = lax.axis_index("group")
    core = lax.axis_index("sub") % 2

    rows_as_block = jnp.zeros((16, block_size), jnp.bfloat16).at[0, :n_parent].set(parent_rows.astype(jnp.bfloat16))
    packed = jnp.concatenate([parent_vals.reshape(n_parent * block_size, block_size), rows_as_block], axis=0)

    onehot = (
        block_cols.reshape(row_blocks, BPR)[:, :, None] == jnp.arange(vertex_blocks)[None, None, :]
    ).astype(jnp.float32)
    blocks = block_vals.astype(jnp.float32).reshape(row_blocks, BPR, block_size, block_size)
    dense = (
        jnp.einsum("rbc,rbij->ricj", onehot, blocks)
        .reshape(row_blocks * block_size, vertex_blocks * block_size)
        .astype(jnp.bfloat16)
    )
    panel = jnp.dot(dense, modes, preferred_element_type=jnp.float32).astype(jnp.bfloat16)
    carried = packed[None]
    for level in range(levels):
        sibling = from_partner(panel, "group", 2**level)
        partner = levels - 1 - level
        carried, panel = lax.optimization_barrier((carried, panel))
        arrived = from_partner(carried, "group", 2**partner)
        total = (panel.astype(jnp.float32) + sibling.astype(jnp.float32)).astype(jnp.bfloat16)
        if level < levels - 1:
            arrived, total = lax.optimization_barrier((arrived, total))
        if level < levels - 1:
            carried = jnp.concatenate([carried, arrived], axis=0)
        else:
            last_arrival = arrived
        mapped = jnp.einsum(
            "ab,rbm->ram",
            level_maps[level],
            total.reshape(row_blocks, block_size, width),
            preferred_element_type=jnp.float32,
        )
        panel = mapped.reshape(row_blocks * block_size, width).astype(jnp.bfloat16)
    quarter = width // merged
    half_rows = block_size // 2
    column = (group_index % merged) * quarter
    head = lax.dynamic_slice_in_dim(panel[:block_size], column, quarter, 1)
    outgoing = jnp.tile(head.reshape(2, half_rows, quarter), (n_sub // 2, 1, 1))

    half = width // 2
    keep_cols = lax.dynamic_slice_in_dim(panel, core * half, half, 1)
    send_cols = lax.dynamic_slice_in_dim(panel, (1 - core) * half, half, 1)
    contract = (((0,), (0,)), ((), ()))
    keep = lax.dot_general(psi, keep_cols, contract, preferred_element_type=jnp.float32)
    send = lax.dot_general(psi, send_cols, contract, preferred_element_type=jnp.float32)
    chip_sum = (keep + from_partner(send, "sub", 1)).reshape(n_sub, width // n_sub, half)
    high = lax.reduce_precision(chip_sum, exponent_bits=8, mantissa_bits=7)
    low = chip_sum - high
    split = jnp.stack([high.astype(jnp.bfloat16), low.astype(jnp.bfloat16)], axis=1).reshape(n_sub, -1, quarter)
    outgoing = jnp.concatenate([outgoing, split], axis=1)
    last_arrival, outgoing = lax.optimization_barrier((last_arrival, outgoing))
    arrived = lax.all_to_all(outgoing, "sub", 0, 0, tiled=True)
    carried = jnp.concatenate([carried, last_arrival], axis=0)
    vals_all = carried[:, : n_parent * block_size].reshape(-1, block_size, block_size)
    rows_all = carried[:, n_parent * block_size, :n_parent].reshape(-1).astype(jnp.int32)
    mine = arrived[:, :half_rows]
    parts = arrived[:, half_rows:].reshape(n_sub, 2, width // n_sub, half).astype(jnp.float32)
    spread = parts[:, 0] + parts[:, 1]
    by_half = spread.reshape(n_sub // 2, 2, width // n_sub, half).sum(axis=0)
    projected = by_half.transpose(1, 0, 2).reshape(width // n_sub, width)

    theirs = from_partner(mine, "sub", 1)
    picked_mine = jnp.take(mine, rows_all, axis=0)
    picked_theirs = jnp.take(theirs, rows_all, axis=0)
    picked_low = jnp.where(core == 0, picked_mine, picked_theirs)
    picked_high = jnp.where(core == 0, picked_theirs, picked_mine)
    parent_sum = jnp.einsum(
        "kab,kbm->am", vals_all[:, :, :half_rows], picked_low, preferred_element_type=jnp.float32
    ) + jnp.einsum("kab,kbm->am", vals_all[:, :, half_rows:], picked_high, preferred_element_type=jnp.float32)
    parent_out = parent_sum.astype(jnp.bfloat16)
    return (parent_out, projected)


def solution(mesh):
    return jax.shard_map(
        on_device,
        mesh=mesh,
        in_specs=(
            P(("group", "sub"), None),
            P(("group", "sub"), None, None),
            P(("group", "sub")),
            P(),
            P(("group", "sub"), None),
            P(("group", "sub"), None, None),
            P(("group", "sub")),
        ),
        out_specs=(P("sub", "group"), P(("group", "sub"), None)),
        check_vma=False,
    )
```

```python
import jax
import jax.numpy as jnp
from jax import lax
from jax.sharding import PartitionSpec as P

IFB = 8
BPR = 6


def from_partner(value, axis, mask):
    pairs = [(source, source ^ mask) for source in range(lax.axis_size(axis))]
    return lax.ppermute(value, axis, pairs)


def on_device(modes, block_vals, block_cols, level_maps, psi, parent_vals, parent_rows):
    block_size = block_vals.shape[1]
    width = modes.shape[1]
    vertex_blocks = modes.shape[0] // block_size
    row_blocks = IFB
    levels = min(2, lax.axis_size("group").bit_length() - 1)
    merged = 2**levels
    n_sub = lax.axis_size("sub")
    n_parent = parent_vals.shape[0]
    group_index = lax.axis_index("group")
    core = lax.axis_index("sub") % 2

    rows_as_block = jnp.zeros((16, block_size), jnp.bfloat16).at[0, :n_parent].set(parent_rows.astype(jnp.bfloat16))
    packed = jnp.concatenate([parent_vals.reshape(n_parent * block_size, block_size), rows_as_block], axis=0)

    onehot = (
        block_cols.reshape(row_blocks, BPR)[:, :, None] == jnp.arange(vertex_blocks)[None, None, :]
    ).astype(jnp.float32)
    blocks = block_vals.astype(jnp.float32).reshape(row_blocks, BPR, block_size, block_size)
    dense = (
        jnp.einsum("rbc,rbij->ricj", onehot, blocks)
        .reshape(row_blocks * block_size, vertex_blocks * block_size)
        .astype(jnp.bfloat16)
    )
    panel = jnp.dot(dense, modes, preferred_element_type=jnp.float32).astype(jnp.bfloat16)
    packed, panel = lax.optimization_barrier((packed, panel))
    held = [packed]
    for level in range(levels):
        sibling = from_partner(panel, "group", 2**level)
        if level == 0:
            sent = [from_partner(packed, "group", 2**lev) for lev in range(levels)]
        else:
            relay, panel = lax.optimization_barrier((held[1], panel))
            sent = [from_partner(relay, "group", 2**level)]
        total = (panel.astype(jnp.float32) + sibling.astype(jnp.float32)).astype(jnp.bfloat16)
        if level < levels - 1:
            sent, total = lax.optimization_barrier((sent, total))
        held = held + sent
        mapped = jnp.einsum(
            "ab,rbm->ram",
            level_maps[level],
            total.reshape(row_blocks, block_size, width),
            preferred_element_type=jnp.float32,
        )
        panel = mapped.reshape(row_blocks * block_size, width).astype(jnp.bfloat16)
    carried = jnp.stack(held)

    quarter = width // merged
    half_rows = block_size // 2
    column = (group_index % merged) * quarter
    head = lax.dynamic_slice_in_dim(panel[:block_size], column, quarter, 1)
    carried, head = lax.optimization_barrier((carried, head))
    vals_all = carried[:, : n_parent * block_size].reshape(-1, block_size, block_size)
    rows_all = carried[:, n_parent * block_size, :n_parent].reshape(-1).astype(jnp.int32)
    outgoing = jnp.tile(head.reshape(2, half_rows, quarter), (n_sub // 2, 1, 1))

    half = width // 2
    keep_cols = lax.dynamic_slice_in_dim(panel, core * half, half, 1)
    send_cols = lax.dynamic_slice_in_dim(panel, (1 - core) * half, half, 1)
    contract = (((0,), (0,)), ((), ()))
    keep = lax.dot_general(psi, keep_cols, contract, preferred_element_type=jnp.float32)
    send = lax.dot_general(psi, send_cols, contract, preferred_element_type=jnp.float32)
    chip_sum = (keep + from_partner(send, "sub", 1)).reshape(n_sub, width // n_sub, half)
    high = lax.reduce_precision(chip_sum, exponent_bits=8, mantissa_bits=7)
    low = chip_sum - high
    split = jnp.stack([high.astype(jnp.bfloat16), low.astype(jnp.bfloat16)], axis=1).reshape(n_sub, -1, quarter)
    outgoing = jnp.concatenate([outgoing, split], axis=1)
    arrived = lax.all_to_all(outgoing, "sub", 0, 0, tiled=True)
    mine = arrived[:, :half_rows]
    parts = arrived[:, half_rows:].reshape(n_sub, 2, width // n_sub, half).astype(jnp.float32)
    spread = parts[:, 0] + parts[:, 1]
    by_half = spread.reshape(n_sub // 2, 2, width // n_sub, half).sum(axis=0)
    projected = by_half.transpose(1, 0, 2).reshape(width // n_sub, width)

    theirs = from_partner(mine, "sub", 1)
    picked_mine = jnp.take(mine, rows_all, axis=0)
    picked_theirs = jnp.take(theirs, rows_all, axis=0)
    picked_low = jnp.where(core == 0, picked_mine, picked_theirs)
    picked_high = jnp.where(core == 0, picked_theirs, picked_mine)
    parent_sum = jnp.einsum(
        "kab,kbm->am", vals_all[:, :, :half_rows], picked_low, preferred_element_type=jnp.float32
    ) + jnp.einsum("kab,kbm->am", vals_all[:, :, half_rows:], picked_high, preferred_element_type=jnp.float32)
    parent_out = parent_sum.astype(jnp.bfloat16)
    return (parent_out, projected)


def solution(mesh):
    return jax.shard_map(
        on_device,
        mesh=mesh,
        in_specs=(
            P(("group", "sub"), None),
            P(("group", "sub"), None, None),
            P(("group", "sub")),
            P(),
            P(("group", "sub"), None),
            P(("group", "sub"), None, None),
            P(("group", "sub")),
        ),
        out_specs=(P("sub", "group"), P(("group", "sub"), None)),
        check_vma=False,
    )
```

```python
import jax
import jax.numpy as jnp
from jax import lax
from jax.sharding import PartitionSpec as P

IFB = 8
BPR = 6


def from_partner(value, axis, mask):
    pairs = [(source, source ^ mask) for source in range(lax.axis_size(axis))]
    return lax.ppermute(value, axis, pairs)


def on_device(modes, block_vals, block_cols, level_maps, psi, parent_vals, parent_rows):
    block_size = block_vals.shape[1]
    width = modes.shape[1]
    vertex_blocks = modes.shape[0] // block_size
    row_blocks = IFB
    levels = min(2, lax.axis_size("group").bit_length() - 1)
    merged = 2**levels
    n_sub = lax.axis_size("sub")
    n_parent = parent_vals.shape[0]
    group_index = lax.axis_index("group")
    core = lax.axis_index("sub") % 2

    rows_as_block = jnp.zeros((16, block_size), jnp.bfloat16).at[0, :n_parent].set(parent_rows.astype(jnp.bfloat16))
    packed = jnp.concatenate([parent_vals.reshape(n_parent * block_size, block_size), rows_as_block], axis=0)

    onehot = (
        block_cols.reshape(row_blocks, BPR)[:, :, None] == jnp.arange(vertex_blocks)[None, None, :]
    ).astype(jnp.float32)
    blocks = block_vals.astype(jnp.float32).reshape(row_blocks, BPR, block_size, block_size)
    dense = (
        jnp.einsum("rbc,rbij->ricj", onehot, blocks)
        .reshape(row_blocks * block_size, vertex_blocks * block_size)
        .astype(jnp.bfloat16)
    )
    panel = jnp.dot(dense, modes, preferred_element_type=jnp.float32).astype(jnp.bfloat16)
    carried = packed[None]
    for level in range(levels):
        sibling = from_partner(panel, "group", 2**level)
        partner = levels - 1 - level
        carried, panel = lax.optimization_barrier((carried, panel))
        arrived = from_partner(carried, "group", 2**partner)
        total = (panel.astype(jnp.float32) + sibling.astype(jnp.float32)).astype(jnp.bfloat16)
        if level < levels - 1:
            arrived, total = lax.optimization_barrier((arrived, total))
        carried = jnp.concatenate([carried, arrived], axis=0)
        mapped = jnp.einsum(
            "ab,rbm->ram",
            level_maps[level],
            total.reshape(row_blocks, block_size, width),
            preferred_element_type=jnp.float32,
        )
        panel = mapped.reshape(row_blocks * block_size, width).astype(jnp.bfloat16)
    quarter = width // merged
    half_rows = block_size // 2
    column = (group_index % merged) * quarter
    head = lax.dynamic_slice_in_dim(panel[:block_size], column, quarter, 1)
    carried, head = lax.optimization_barrier((carried, head))
    vals_all = carried[:, : n_parent * block_size].reshape(-1, block_size, block_size)
    rows_all = carried[:, n_parent * block_size, :n_parent].reshape(-1).astype(jnp.int32)
    outgoing = jnp.tile(head.reshape(2, half_rows, quarter), (n_sub // 2, 1, 1))

    half = width // 2
    keep_cols = lax.dynamic_slice_in_dim(panel, core * half, half, 1)
    send_cols = lax.dynamic_slice_in_dim(panel, (1 - core) * half, half, 1)
    contract = (((0,), (0,)), ((), ()))
    keep = lax.dot_general(psi, keep_cols, contract, preferred_element_type=jnp.float32)
    send = lax.dot_general(psi, send_cols, contract, preferred_element_type=jnp.float32)
    chip_sum = keep + from_partner(send, "sub", 1)
    lanes = 128
    tiles = half // lanes
    out_rows = width // n_sub
    col_tiles = [chip_sum[:, i * lanes : (i + 1) * lanes].reshape(n_sub, out_rows, lanes) for i in range(tiles)]
    highs = [lax.reduce_precision(t, exponent_bits=8, mantissa_bits=7) for t in col_tiles]
    lows = [t - h for t, h in zip(col_tiles, highs)]
    split = jnp.concatenate([h.astype(jnp.bfloat16) for h in highs] + [l.astype(jnp.bfloat16) for l in lows], axis=1)
    outgoing = jnp.concatenate([outgoing, split.reshape(n_sub, -1, quarter)], axis=1)
    arrived = lax.all_to_all(outgoing, "sub", 0, 0, tiled=True)
    mine = arrived[:, :half_rows]
    parts = arrived[:, half_rows:].astype(jnp.float32).reshape(n_sub, 2 * tiles, out_rows, lanes)
    spread = parts[:, :tiles] + parts[:, tiles:]
    by_half = spread.reshape(n_sub // 2, 2, tiles, out_rows, lanes).sum(axis=0)
    projected = by_half.transpose(2, 0, 1, 3).reshape(out_rows, width)

    theirs = from_partner(mine, "sub", 1)
    picked_mine = jnp.take(mine, rows_all, axis=0)
    picked_theirs = jnp.take(theirs, rows_all, axis=0)
    picked_low = jnp.where(core == 0, picked_mine, picked_theirs)
    picked_high = jnp.where(core == 0, picked_theirs, picked_mine)
    parent_sum = jnp.einsum(
        "kab,kbm->am", vals_all[:, :, :half_rows], picked_low, preferred_element_type=jnp.float32
    ) + jnp.einsum("kab,kbm->am", vals_all[:, :, half_rows:], picked_high, preferred_element_type=jnp.float32)
    parent_out = parent_sum.astype(jnp.bfloat16)
    return (parent_out, projected)


def solution(mesh):
    return jax.shard_map(
        on_device,
        mesh=mesh,
        in_specs=(
            P(("group", "sub"), None),
            P(("group", "sub"), None, None),
            P(("group", "sub")),
            P(),
            P(("group", "sub"), None),
            P(("group", "sub"), None, None),
            P(("group", "sub")),
        ),
        out_specs=(P("sub", "group"), P(("group", "sub"), None)),
        check_vma=False,
    )
```

```python
import jax
import jax.numpy as jnp
from jax import lax
from jax.sharding import PartitionSpec as P

IFB = 8
BPR = 6


def from_partner(value, axis, mask):
    pairs = [(source, source ^ mask) for source in range(lax.axis_size(axis))]
    return lax.ppermute(value, axis, pairs)


def on_device(modes, block_vals, block_cols, level_maps, psi, parent_vals, parent_rows):
    block_size = block_vals.shape[1]
    width = modes.shape[1]
    vertex_blocks = modes.shape[0] // block_size
    row_blocks = IFB
    levels = min(2, lax.axis_size("group").bit_length() - 1)
    merged = 2**levels
    n_sub = lax.axis_size("sub")
    n_parent = parent_vals.shape[0]
    group_index = lax.axis_index("group")
    core = lax.axis_index("sub") % 2

    rows_as_block = jnp.zeros((16, block_size), jnp.bfloat16).at[0, :n_parent].set(parent_rows.astype(jnp.bfloat16))
    packed = jnp.concatenate([parent_vals.reshape(n_parent * block_size, block_size), rows_as_block], axis=0)

    onehot = (
        block_cols.reshape(row_blocks, BPR)[:, :, None] == jnp.arange(vertex_blocks)[None, None, :]
    ).astype(jnp.float32)
    blocks = block_vals.astype(jnp.float32).reshape(row_blocks, BPR, block_size, block_size)
    dense = (
        jnp.einsum("rbc,rbij->ricj", onehot, blocks)
        .reshape(row_blocks * block_size, vertex_blocks * block_size)
        .astype(jnp.bfloat16)
    )
    panel = jnp.dot(dense, modes, preferred_element_type=jnp.float32).astype(jnp.bfloat16)
    carried = packed[None]
    for level in range(levels):
        sibling = from_partner(panel, "group", 2**level)
        partner = levels - 1 - level
        carried, panel = lax.optimization_barrier((carried, panel))
        arrived = from_partner(carried, "group", 2**partner)
        total = (panel.astype(jnp.float32) + sibling.astype(jnp.float32)).astype(jnp.bfloat16)
        if level < levels - 1:
            arrived, total = lax.optimization_barrier((arrived, total))
        carried = jnp.concatenate([carried, arrived], axis=0)
        mapped = jnp.einsum(
            "ab,rbm->ram",
            level_maps[level],
            total.reshape(row_blocks, block_size, width),
            preferred_element_type=jnp.float32,
        )
        panel = mapped.reshape(row_blocks * block_size, width).astype(jnp.bfloat16)
    quarter = width // merged
    half_rows = block_size // 2
    column = (group_index % merged) * quarter
    head = lax.dynamic_slice_in_dim(panel[:block_size], column, quarter, 1)
    vals_all = carried[:, : n_parent * block_size].reshape(-1, block_size, block_size)
    rows_all = carried[:, n_parent * block_size, :n_parent].reshape(-1).astype(jnp.int32)

    half = width // 2
    keep_cols = lax.dynamic_slice_in_dim(panel, core * half, half, 1)
    send_cols = lax.dynamic_slice_in_dim(panel, (1 - core) * half, half, 1)
    contract = (((0,), (0,)), ((), ()))
    keep = lax.dot_general(psi, keep_cols, contract, preferred_element_type=jnp.float32)
    send = lax.dot_general(psi, send_cols, contract, preferred_element_type=jnp.float32)
    chip_sum = keep + from_partner(send, "sub", 1)
    lanes = 128
    tiles = half // lanes
    out_rows = width // n_sub
    col_tiles = [chip_sum[:, i * lanes : (i + 1) * lanes].reshape(n_sub, out_rows, lanes) for i in range(tiles)]
    highs = [lax.reduce_precision(t, exponent_bits=8, mantissa_bits=7) for t in col_tiles]
    lows = [t - h for t, h in zip(col_tiles, highs)]
    split = jnp.concatenate([h.astype(jnp.bfloat16) for h in highs] + [l.astype(jnp.bfloat16) for l in lows], axis=1)
    carried, head, split = lax.optimization_barrier((carried, head, split))
    outgoing = jnp.tile(head.reshape(2, half_rows, quarter), (n_sub // 2, 1, 1))
    outgoing = jnp.concatenate([outgoing, split.reshape(n_sub, -1, quarter)], axis=1)
    arrived = lax.all_to_all(outgoing, "sub", 0, 0, tiled=True)
    mine = arrived[:, :half_rows]
    parts = arrived[:, half_rows:].astype(jnp.float32).reshape(n_sub, 2 * tiles, out_rows, lanes)
    spread = parts[:, :tiles] + parts[:, tiles:]
    by_half = spread.reshape(n_sub // 2, 2, tiles, out_rows, lanes).sum(axis=0)
    projected = by_half.transpose(2, 0, 1, 3).reshape(out_rows, width)

    theirs = from_partner(mine, "sub", 1)
    picked_mine = jnp.take(mine, rows_all, axis=0)
    picked_theirs = jnp.take(theirs, rows_all, axis=0)
    picked_low = jnp.where(core == 0, picked_mine, picked_theirs)
    picked_high = jnp.where(core == 0, picked_theirs, picked_mine)
    parent_sum = jnp.einsum(
        "kab,kbm->am", vals_all[:, :, :half_rows], picked_low, preferred_element_type=jnp.float32
    ) + jnp.einsum("kab,kbm->am", vals_all[:, :, half_rows:], picked_high, preferred_element_type=jnp.float32)
    parent_out = parent_sum.astype(jnp.bfloat16)
    return (parent_out, projected)


def solution(mesh):
    return jax.shard_map(
        on_device,
        mesh=mesh,
        in_specs=(
            P(("group", "sub"), None),
            P(("group", "sub"), None, None),
            P(("group", "sub")),
            P(),
            P(("group", "sub"), None),
            P(("group", "sub"), None, None),
            P(("group", "sub")),
        ),
        out_specs=(P("sub", "group"), P(("group", "sub"), None)),
        check_vma=False,
    )
```

```python
import jax
import jax.numpy as jnp
from jax import lax
from jax.sharding import PartitionSpec as P

IFB = 8
BPR = 6


def from_partner(value, axis, mask):
    pairs = [(source, source ^ mask) for source in range(lax.axis_size(axis))]
    return lax.ppermute(value, axis, pairs)


def on_device(modes, block_vals, block_cols, level_maps, psi, parent_vals, parent_rows):
    block_size = block_vals.shape[1]
    width = modes.shape[1]
    vertex_blocks = modes.shape[0] // block_size
    row_blocks = IFB
    levels = min(2, lax.axis_size("group").bit_length() - 1)
    merged = 2**levels
    n_sub = lax.axis_size("sub")
    n_parent = parent_vals.shape[0]
    group_index = lax.axis_index("group")
    core = lax.axis_index("sub") % 2

    rows_as_block = jnp.zeros((16, block_size), jnp.bfloat16).at[0, :n_parent].set(parent_rows.astype(jnp.bfloat16))
    packed = jnp.concatenate([parent_vals.reshape(n_parent * block_size, block_size), rows_as_block], axis=0)

    onehot = (
        block_cols.reshape(row_blocks, BPR)[:, :, None] == jnp.arange(vertex_blocks)[None, None, :]
    ).astype(jnp.float32)
    blocks = block_vals.astype(jnp.float32).reshape(row_blocks, BPR, block_size, block_size)
    dense = (
        jnp.einsum("rbc,rbij->ricj", onehot, blocks)
        .reshape(row_blocks * block_size, vertex_blocks * block_size)
        .astype(jnp.bfloat16)
    )
    panel = jnp.dot(dense, modes, preferred_element_type=jnp.float32).astype(jnp.bfloat16)
    carried = packed[None]
    for level in range(levels):
        sibling = from_partner(panel, "group", 2**level)
        partner = levels - 1 - level
        carried, panel = lax.optimization_barrier((carried, panel))
        outbound = carried if level < levels - 1 else carried[:1]
        arrived = from_partner(outbound, "group", 2**partner)
        total = (panel.astype(jnp.float32) + sibling.astype(jnp.float32)).astype(jnp.bfloat16)
        if level < levels - 1:
            arrived, total = lax.optimization_barrier((arrived, total))
        carried = jnp.concatenate([carried, arrived], axis=0)
        mapped = jnp.einsum(
            "ab,rbm->ram",
            level_maps[level],
            total.reshape(row_blocks, block_size, width),
            preferred_element_type=jnp.float32,
        )
        panel = mapped.reshape(row_blocks * block_size, width).astype(jnp.bfloat16)
    quarter = width // merged
    half_rows = block_size // 2
    column = (group_index % merged) * quarter
    head = lax.dynamic_slice_in_dim(panel[:block_size], column, quarter, 1)

    half = width // 2
    keep_cols = lax.dynamic_slice_in_dim(panel, core * half, half, 1)
    send_cols = lax.dynamic_slice_in_dim(panel, (1 - core) * half, half, 1)
    contract = (((0,), (0,)), ((), ()))
    keep = lax.dot_general(psi, keep_cols, contract, preferred_element_type=jnp.float32)
    send = lax.dot_general(psi, send_cols, contract, preferred_element_type=jnp.float32)
    chip_sum = keep + from_partner(send, "sub", 1)
    lanes = 128
    tiles = half // lanes
    out_rows = width // n_sub
    col_tiles = [chip_sum[:, i * lanes : (i + 1) * lanes].reshape(n_sub, out_rows, lanes) for i in range(tiles)]
    highs = [lax.reduce_precision(t, exponent_bits=8, mantissa_bits=7) for t in col_tiles]
    lows = [t - h for t, h in zip(col_tiles, highs)]
    split = jnp.concatenate([h.astype(jnp.bfloat16) for h in highs] + [l.astype(jnp.bfloat16) for l in lows], axis=1)
    carried, head, split = lax.optimization_barrier((carried, head, split))
    relayed = from_partner(carried[-1:], "group", 2 ** (levels - 1))
    carried = jnp.concatenate([carried, relayed], axis=0)
    vals_all = carried[:, : n_parent * block_size].reshape(-1, block_size, block_size)
    rows_all = carried[:, n_parent * block_size, :n_parent].reshape(-1).astype(jnp.int32)
    outgoing = jnp.tile(head.reshape(2, half_rows, quarter), (n_sub // 2, 1, 1))
    outgoing = jnp.concatenate([outgoing, split.reshape(n_sub, -1, quarter)], axis=1)
    arrived = lax.all_to_all(outgoing, "sub", 0, 0, tiled=True)
    mine = arrived[:, :half_rows]
    parts = arrived[:, half_rows:].astype(jnp.float32).reshape(n_sub, 2 * tiles, out_rows, lanes)
    spread = parts[:, :tiles] + parts[:, tiles:]
    by_half = spread.reshape(n_sub // 2, 2, tiles, out_rows, lanes).sum(axis=0)
    projected = by_half.transpose(2, 0, 1, 3).reshape(out_rows, width)

    theirs = from_partner(mine, "sub", 1)
    picked_mine = jnp.take(mine, rows_all, axis=0)
    picked_theirs = jnp.take(theirs, rows_all, axis=0)
    picked_low = jnp.where(core == 0, picked_mine, picked_theirs)
    picked_high = jnp.where(core == 0, picked_theirs, picked_mine)
    parent_sum = jnp.einsum(
        "kab,kbm->am", vals_all[:, :, :half_rows], picked_low, preferred_element_type=jnp.float32
    ) + jnp.einsum("kab,kbm->am", vals_all[:, :, half_rows:], picked_high, preferred_element_type=jnp.float32)
    parent_out = parent_sum.astype(jnp.bfloat16)
    return (parent_out, projected)


def solution(mesh):
    return jax.shard_map(
        on_device,
        mesh=mesh,
        in_specs=(
            P(("group", "sub"), None),
            P(("group", "sub"), None, None),
            P(("group", "sub")),
            P(),
            P(("group", "sub"), None),
            P(("group", "sub"), None, None),
            P(("group", "sub")),
        ),
        out_specs=(P("sub", "group"), P(("group", "sub"), None)),
        check_vma=False,
    )
```

```python
import jax
import jax.numpy as jnp
from jax import lax
from jax.sharding import PartitionSpec as P

IFB = 8
BPR = 6


def from_partner(value, axis, mask):
    pairs = [(source, source ^ mask) for source in range(lax.axis_size(axis))]
    return lax.ppermute(value, axis, pairs)


def on_device(modes, block_vals, block_cols, level_maps, psi, parent_vals, parent_rows):
    block_size = block_vals.shape[1]
    width = modes.shape[1]
    vertex_blocks = modes.shape[0] // block_size
    row_blocks = IFB
    levels = min(2, lax.axis_size("group").bit_length() - 1)
    merged = 2**levels
    n_sub = lax.axis_size("sub")
    n_parent = parent_vals.shape[0]
    group_index = lax.axis_index("group")
    core = lax.axis_index("sub") % 2

    rows_as_block = jnp.zeros((16, block_size), jnp.bfloat16).at[0, :n_parent].set(parent_rows.astype(jnp.bfloat16))
    packed = jnp.concatenate([parent_vals.reshape(n_parent * block_size, block_size), rows_as_block], axis=0)

    onehot = (
        block_cols.reshape(row_blocks, BPR)[:, :, None] == jnp.arange(vertex_blocks)[None, None, :]
    ).astype(jnp.float32)
    blocks = block_vals.astype(jnp.float32).reshape(row_blocks, BPR, block_size, block_size)
    dense = (
        jnp.einsum("rbc,rbij->ricj", onehot, blocks)
        .reshape(row_blocks * block_size, vertex_blocks * block_size)
        .astype(jnp.bfloat16)
    )
    panel = jnp.dot(dense, modes, preferred_element_type=jnp.float32).astype(jnp.bfloat16)
    carried = packed[None]
    for level in range(levels):
        sibling = from_partner(panel, "group", 2**level)
        partner = levels - 1 - level
        carried, panel = lax.optimization_barrier((carried, panel))
        arrived = from_partner(carried, "group", 2**partner)
        total = (panel.astype(jnp.float32) + sibling.astype(jnp.float32)).astype(jnp.bfloat16)
        if level < levels - 1:
            arrived, total = lax.optimization_barrier((arrived, total))
        carried = jnp.concatenate([carried, arrived], axis=0)
        mapped = jnp.einsum(
            "ab,rbm->ram",
            level_maps[level],
            total.reshape(row_blocks, block_size, width),
            preferred_element_type=jnp.float32,
        )
        panel = mapped.reshape(row_blocks * block_size, width).astype(jnp.bfloat16)
    quarter = width // merged
    half_rows = block_size // 2
    column = (group_index % merged) * quarter
    head = lax.dynamic_slice_in_dim(panel[:block_size], column, quarter, 1)
    vals_all = carried[:, : n_parent * block_size].reshape(-1, block_size, block_size)
    rows_all = carried[:, n_parent * block_size, :n_parent].reshape(-1).astype(jnp.int32)

    half = width // 2
    keep_cols = lax.dynamic_slice_in_dim(panel, core * half, half, 1)
    send_cols = lax.dynamic_slice_in_dim(panel, (1 - core) * half, half, 1)
    contract = (((0,), (0,)), ((), ()))
    keep = lax.dot_general(psi, keep_cols, contract, preferred_element_type=jnp.float32)
    send = lax.dot_general(psi, send_cols, contract, preferred_element_type=jnp.float32)
    chip_sum = keep + from_partner(send, "sub", 1)
    lanes = 128
    tiles = half // lanes
    out_rows = width // n_sub
    col_tiles = [chip_sum[:, i * lanes : (i + 1) * lanes].reshape(n_sub, out_rows, lanes) for i in range(tiles)]
    highs = [lax.reduce_precision(t, exponent_bits=8, mantissa_bits=7) for t in col_tiles]
    lows = [t - h for t, h in zip(col_tiles, highs)]
    split = jnp.concatenate([h.astype(jnp.bfloat16) for h in highs] + [l.astype(jnp.bfloat16) for l in lows], axis=1)
    vals_all, rows_all, head, split = lax.optimization_barrier((vals_all, rows_all, head, split))
    outgoing = jnp.tile(head.reshape(2, half_rows, quarter), (n_sub // 2, 1, 1))
    outgoing = jnp.concatenate([outgoing, split.reshape(n_sub, -1, quarter)], axis=1)
    arrived = lax.all_to_all(outgoing, "sub", 0, 0, tiled=True)
    mine = arrived[:, :half_rows]
    parts = arrived[:, half_rows:].astype(jnp.float32).reshape(n_sub, 2 * tiles, out_rows, lanes)
    spread = parts[:, :tiles] + parts[:, tiles:]
    by_half = spread.reshape(n_sub // 2, 2, tiles, out_rows, lanes).sum(axis=0)
    projected = by_half.transpose(2, 0, 1, 3).reshape(out_rows, width)

    theirs = from_partner(arrived, "sub", 1)
    picked_mine = jnp.take(arrived, rows_all, axis=0)[:, :half_rows]
    picked_theirs = jnp.take(theirs, rows_all, axis=0)[:, :half_rows]
    picked_low = jnp.where(core == 0, picked_mine, picked_theirs)
    picked_high = jnp.where(core == 0, picked_theirs, picked_mine)
    parent_sum = jnp.einsum(
        "kab,kbm->am", vals_all[:, :, :half_rows], picked_low, preferred_element_type=jnp.float32
    ) + jnp.einsum("kab,kbm->am", vals_all[:, :, half_rows:], picked_high, preferred_element_type=jnp.float32)
    parent_out = parent_sum.astype(jnp.bfloat16)
    return (parent_out, projected)


def solution(mesh):
    return jax.shard_map(
        on_device,
        mesh=mesh,
        in_specs=(
            P(("group", "sub"), None),
            P(("group", "sub"), None, None),
            P(("group", "sub")),
            P(),
            P(("group", "sub"), None),
            P(("group", "sub"), None, None),
            P(("group", "sub")),
        ),
        out_specs=(P("sub", "group"), P(("group", "sub"), None)),
        check_vma=False,
    )
```

```python
import jax
import jax.numpy as jnp
from jax import lax
from jax.sharding import PartitionSpec as P

IFB = 8
BPR = 6


def from_partner(value, axis, mask):
    pairs = [(source, source ^ mask) for source in range(lax.axis_size(axis))]
    return lax.ppermute(value, axis, pairs)


def on_device(modes, block_vals, block_cols, level_maps, psi, parent_vals, parent_rows):
    block_size = block_vals.shape[1]
    width = modes.shape[1]
    vertex_blocks = modes.shape[0] // block_size
    row_blocks = IFB
    levels = min(2, lax.axis_size("group").bit_length() - 1)
    merged = 2**levels
    n_sub = lax.axis_size("sub")
    n_parent = parent_vals.shape[0]
    group_index = lax.axis_index("group")
    core = lax.axis_index("sub") % 2

    rows_as_block = jnp.zeros((16, block_size), jnp.bfloat16).at[0, :n_parent].set(parent_rows.astype(jnp.bfloat16))
    packed = jnp.concatenate([parent_vals.reshape(n_parent * block_size, block_size), rows_as_block], axis=0)

    onehot = (
        block_cols.reshape(row_blocks, BPR)[:, :, None] == jnp.arange(vertex_blocks)[None, None, :]
    ).astype(jnp.float32)
    blocks = block_vals.astype(jnp.float32).reshape(row_blocks, BPR, block_size, block_size)
    dense = (
        jnp.einsum("rbc,rbij->ricj", onehot, blocks)
        .reshape(row_blocks * block_size, vertex_blocks * block_size)
        .astype(jnp.bfloat16)
    )
    panel = jnp.dot(dense, modes, preferred_element_type=jnp.float32).astype(jnp.bfloat16)
    carried = packed[None]
    for level in range(levels):
        if level == 0:
            sibling = from_partner(panel, "group", 2**level)
        else:
            rows_half = panel.shape[0] // 2
            sibling = jnp.concatenate(
                [from_partner(panel[:rows_half], "group", 2**level), from_partner(panel[rows_half:], "group", 2**level)]
            )
        partner = levels - 1 - level
        carried, panel = lax.optimization_barrier((carried, panel))
        arrived = from_partner(carried, "group", 2**partner)
        total = (panel.astype(jnp.float32) + sibling.astype(jnp.float32)).astype(jnp.bfloat16)
        if level < levels - 1:
            arrived, total = lax.optimization_barrier((arrived, total))
        carried = jnp.concatenate([carried, arrived], axis=0)
        mapped = jnp.einsum(
            "ab,rbm->ram",
            level_maps[level],
            total.reshape(row_blocks, block_size, width),
            preferred_element_type=jnp.float32,
        )
        panel = mapped.reshape(row_blocks * block_size, width).astype(jnp.bfloat16)
    quarter = width // merged
    half_rows = block_size // 2
    column = (group_index % merged) * quarter
    head = lax.dynamic_slice_in_dim(panel[:block_size], column, quarter, 1)
    vals_all = carried[:, : n_parent * block_size].reshape(-1, block_size, block_size)
    rows_all = carried[:, n_parent * block_size, :n_parent].reshape(-1).astype(jnp.int32)

    half = width // 2
    keep_cols = lax.dynamic_slice_in_dim(panel, core * half, half, 1)
    send_cols = lax.dynamic_slice_in_dim(panel, (1 - core) * half, half, 1)
    contract = (((0,), (0,)), ((), ()))
    keep = lax.dot_general(psi, keep_cols, contract, preferred_element_type=jnp.float32)
    send = lax.dot_general(psi, send_cols, contract, preferred_element_type=jnp.float32)
    chip_sum = keep + from_partner(send, "sub", 1)
    lanes = 128
    tiles = half // lanes
    out_rows = width // n_sub
    col_tiles = [chip_sum[:, i * lanes : (i + 1) * lanes].reshape(n_sub, out_rows, lanes) for i in range(tiles)]
    highs = [lax.reduce_precision(t, exponent_bits=8, mantissa_bits=7) for t in col_tiles]
    lows = [t - h for t, h in zip(col_tiles, highs)]
    split = jnp.concatenate([h.astype(jnp.bfloat16) for h in highs] + [l.astype(jnp.bfloat16) for l in lows], axis=1)
    carried, head, split = lax.optimization_barrier((carried, head, split))
    outgoing = jnp.tile(head.reshape(2, half_rows, quarter), (n_sub // 2, 1, 1))
    outgoing = jnp.concatenate([outgoing, split.reshape(n_sub, -1, quarter)], axis=1)
    arrived = lax.all_to_all(outgoing, "sub", 0, 0, tiled=True)
    mine = arrived[:, :half_rows]
    parts = arrived[:, half_rows:].astype(jnp.float32).reshape(n_sub, 2 * tiles, out_rows, lanes)
    spread = parts[:, :tiles] + parts[:, tiles:]
    by_half = spread.reshape(n_sub // 2, 2, tiles, out_rows, lanes).sum(axis=0)
    projected = by_half.transpose(2, 0, 1, 3).reshape(out_rows, width)

    theirs = from_partner(mine, "sub", 1)
    picked_mine = jnp.take(mine, rows_all, axis=0)
    picked_theirs = jnp.take(theirs, rows_all, axis=0)
    picked_low = jnp.where(core == 0, picked_mine, picked_theirs)
    picked_high = jnp.where(core == 0, picked_theirs, picked_mine)
    parent_sum = jnp.einsum(
        "kab,kbm->am", vals_all[:, :, :half_rows], picked_low, preferred_element_type=jnp.float32
    ) + jnp.einsum("kab,kbm->am", vals_all[:, :, half_rows:], picked_high, preferred_element_type=jnp.float32)
    parent_out = parent_sum.astype(jnp.bfloat16)
    return (parent_out, projected)


def solution(mesh):
    return jax.shard_map(
        on_device,
        mesh=mesh,
        in_specs=(
            P(("group", "sub"), None),
            P(("group", "sub"), None, None),
            P(("group", "sub")),
            P(),
            P(("group", "sub"), None),
            P(("group", "sub"), None, None),
            P(("group", "sub")),
        ),
        out_specs=(P("sub", "group"), P(("group", "sub"), None)),
        check_vma=False,
    )
```

```python
import jax
import jax.numpy as jnp
from jax import lax
from jax.sharding import PartitionSpec as P

IFB = 8
BPR = 6


def from_partner(value, axis, mask):
    pairs = [(source, source ^ mask) for source in range(lax.axis_size(axis))]
    return lax.ppermute(value, axis, pairs)


def on_device(modes, block_vals, block_cols, level_maps, psi, parent_vals, parent_rows):
    block_size = block_vals.shape[1]
    width = modes.shape[1]
    vertex_blocks = modes.shape[0] // block_size
    row_blocks = IFB
    levels = min(2, lax.axis_size("group").bit_length() - 1)
    merged = 2**levels
    n_sub = lax.axis_size("sub")
    n_parent = parent_vals.shape[0]
    group_index = lax.axis_index("group")
    core = lax.axis_index("sub") % 2

    rows_as_block = jnp.zeros((16, block_size), jnp.bfloat16).at[0, :n_parent].set(parent_rows.astype(jnp.bfloat16))
    packed = jnp.concatenate([parent_vals.reshape(n_parent * block_size, block_size), rows_as_block], axis=0)

    onehot = (
        block_cols.reshape(row_blocks, BPR)[:, :, None] == jnp.arange(vertex_blocks)[None, None, :]
    ).astype(jnp.float32)
    blocks = block_vals.astype(jnp.float32).reshape(row_blocks, BPR, block_size, block_size)
    dense = (
        jnp.einsum("rbc,rbij->ricj", onehot, blocks)
        .reshape(row_blocks * block_size, vertex_blocks * block_size)
        .astype(jnp.bfloat16)
    )
    panel = jnp.dot(dense, modes, preferred_element_type=jnp.float32).astype(jnp.bfloat16)
    carried = packed[None]
    for level in range(levels):
        sibling = from_partner(panel, "group", 2**level)
        partner = levels - 1 - level
        carried, panel = lax.optimization_barrier((carried, panel))
        arrived = from_partner(carried, "group", 2**partner)
        total = (panel.astype(jnp.float32) + sibling.astype(jnp.float32)).astype(jnp.bfloat16)
        if level < levels - 1:
            arrived, total = lax.optimization_barrier((arrived, total))
        carried = jnp.concatenate([carried, arrived], axis=0)
        mapped = jnp.einsum(
            "ab,rbm->ram",
            level_maps[level],
            total.reshape(row_blocks, block_size, width),
            preferred_element_type=jnp.float32,
        )
        panel = mapped.reshape(row_blocks * block_size, width).astype(jnp.bfloat16)
    quarter = width // merged
    half_rows = block_size // 2
    column = (group_index % merged) * quarter
    head = lax.dynamic_slice_in_dim(panel[:block_size], column, quarter, 1)
    vals_all = carried[:, : n_parent * block_size].reshape(-1, block_size, block_size)
    rows_all = carried[:, n_parent * block_size, :n_parent].reshape(-1).astype(jnp.int32)

    half = width // 2
    keep_cols = lax.dynamic_slice_in_dim(panel, core * half, half, 1)
    send_cols = lax.dynamic_slice_in_dim(panel, (1 - core) * half, half, 1)
    contract = (((0,), (0,)), ((), ()))
    keep = lax.dot_general(psi, keep_cols, contract, preferred_element_type=jnp.float32)
    send = lax.dot_general(psi, send_cols, contract, preferred_element_type=jnp.float32)
    chip_sum = keep + from_partner(send, "sub", 1)
    lanes = 128
    tiles = half // lanes
    out_rows = width // n_sub
    col_tiles = [chip_sum[:, i * lanes : (i + 1) * lanes].reshape(n_sub, out_rows, lanes) for i in range(tiles)]
    highs = [lax.reduce_precision(t, exponent_bits=8, mantissa_bits=7) for t in col_tiles]
    lows = [t - h for t, h in zip(col_tiles, highs)]
    split = jnp.concatenate([h.astype(jnp.bfloat16) for h in highs] + [l.astype(jnp.bfloat16) for l in lows], axis=1)
    carried, head, split = lax.optimization_barrier((carried, head, split))
    outgoing = jnp.tile(head.reshape(2, half_rows, quarter), (n_sub // 2, 1, 1))
    outgoing = jnp.concatenate([outgoing, split.reshape(n_sub, -1, quarter)], axis=1)
    arrived = lax.all_to_all(outgoing, "sub", 0, 0, tiled=True)
    mine = arrived[:, :half_rows]
    parts = arrived[:, half_rows:].astype(jnp.float32).reshape(n_sub, 2 * tiles, out_rows, lanes)
    spread = parts[:, :tiles] + parts[:, tiles:]
    by_half = spread.reshape(n_sub // 2, 2, tiles, out_rows, lanes).sum(axis=0)
    projected = by_half.transpose(2, 0, 1, 3).reshape(out_rows, width)

    theirs = from_partner(mine, "sub", 1)
    picked_mine = jnp.take(mine, rows_all, axis=0)
    picked_theirs = jnp.take(theirs, rows_all, axis=0)
    picked_low = jnp.where(core == 0, picked_mine, picked_theirs)
    picked_high = jnp.where(core == 0, picked_theirs, picked_mine)
    picked = jnp.concatenate([picked_low, picked_high], axis=1)
    parent_sum = jnp.einsum("kab,kbm->am", vals_all, picked, preferred_element_type=jnp.float32)
    parent_out = parent_sum.astype(jnp.bfloat16)
    return (parent_out, projected)


def solution(mesh):
    return jax.shard_map(
        on_device,
        mesh=mesh,
        in_specs=(
            P(("group", "sub"), None),
            P(("group", "sub"), None, None),
            P(("group", "sub")),
            P(),
            P(("group", "sub"), None),
            P(("group", "sub"), None, None),
            P(("group", "sub")),
        ),
        out_specs=(P("sub", "group"), P(("group", "sub"), None)),
        check_vma=False,
    )
```

```python
import jax
import jax.numpy as jnp
from jax import lax
from jax.sharding import PartitionSpec as P

IFB = 8
BPR = 6


def from_partner(value, axis, mask):
    pairs = [(source, source ^ mask) for source in range(lax.axis_size(axis))]
    return lax.ppermute(value, axis, pairs)


def on_device(modes, block_vals, block_cols, level_maps, psi, parent_vals, parent_rows):
    block_size = block_vals.shape[1]
    width = modes.shape[1]
    vertex_blocks = modes.shape[0] // block_size
    row_blocks = IFB
    levels = min(2, lax.axis_size("group").bit_length() - 1)
    merged = 2**levels
    n_sub = lax.axis_size("sub")
    n_parent = parent_vals.shape[0]
    group_index = lax.axis_index("group")
    core = lax.axis_index("sub") % 2

    rows_as_block = jnp.zeros((16, block_size), jnp.bfloat16).at[0, :n_parent].set(parent_rows.astype(jnp.bfloat16))
    packed = jnp.concatenate([parent_vals.reshape(n_parent * block_size, block_size), rows_as_block], axis=0)

    onehot = (
        block_cols.reshape(row_blocks, BPR)[:, :, None] == jnp.arange(vertex_blocks)[None, None, :]
    ).astype(jnp.float32)
    blocks = block_vals.astype(jnp.float32).reshape(row_blocks, BPR, block_size, block_size)
    dense = (
        jnp.einsum("rbc,rbij->ricj", onehot, blocks)
        .reshape(row_blocks * block_size, vertex_blocks * block_size)
        .astype(jnp.bfloat16)
    )
    rows_half = dense.shape[0] // 2
    panel_parts = [
        jnp.dot(dense[i * rows_half : (i + 1) * rows_half], modes, preferred_element_type=jnp.float32).astype(jnp.bfloat16)
        for i in range(2)
    ]
    panel = jnp.concatenate(panel_parts, axis=0)
    carried = packed[None]
    for level in range(levels):
        if level == 0:
            sibling = jnp.concatenate([from_partner(p, "group", 2**level) for p in panel_parts], axis=0)
        else:
            sibling = from_partner(panel, "group", 2**level)
        partner = levels - 1 - level
        carried, panel = lax.optimization_barrier((carried, panel))
        arrived = from_partner(carried, "group", 2**partner)
        total = (panel.astype(jnp.float32) + sibling.astype(jnp.float32)).astype(jnp.bfloat16)
        if level < levels - 1:
            arrived, total = lax.optimization_barrier((arrived, total))
        carried = jnp.concatenate([carried, arrived], axis=0)
        mapped = jnp.einsum(
            "ab,rbm->ram",
            level_maps[level],
            total.reshape(row_blocks, block_size, width),
            preferred_element_type=jnp.float32,
        )
        panel = mapped.reshape(row_blocks * block_size, width).astype(jnp.bfloat16)
    quarter = width // merged
    half_rows = block_size // 2
    column = (group_index % merged) * quarter
    head = lax.dynamic_slice_in_dim(panel[:block_size], column, quarter, 1)
    vals_all = carried[:, : n_parent * block_size].reshape(-1, block_size, block_size)
    rows_all = carried[:, n_parent * block_size, :n_parent].reshape(-1).astype(jnp.int32)

    half = width // 2
    keep_cols = lax.dynamic_slice_in_dim(panel, core * half, half, 1)
    send_cols = lax.dynamic_slice_in_dim(panel, (1 - core) * half, half, 1)
    contract = (((0,), (0,)), ((), ()))
    keep = lax.dot_general(psi, keep_cols, contract, preferred_element_type=jnp.float32)
    send = lax.dot_general(psi, send_cols, contract, preferred_element_type=jnp.float32)
    chip_sum = keep + from_partner(send, "sub", 1)
    lanes = 128
    tiles = half // lanes
    out_rows = width // n_sub
    col_tiles = [chip_sum[:, i * lanes : (i + 1) * lanes].reshape(n_sub, out_rows, lanes) for i in range(tiles)]
    highs = [lax.reduce_precision(t, exponent_bits=8, mantissa_bits=7) for t in col_tiles]
    lows = [t - h for t, h in zip(col_tiles, highs)]
    split = jnp.concatenate([h.astype(jnp.bfloat16) for h in highs] + [l.astype(jnp.bfloat16) for l in lows], axis=1)
    carried, head, split = lax.optimization_barrier((carried, head, split))
    outgoing = jnp.tile(head.reshape(2, half_rows, quarter), (n_sub // 2, 1, 1))
    outgoing = jnp.concatenate([outgoing, split.reshape(n_sub, -1, quarter)], axis=1)
    arrived = lax.all_to_all(outgoing, "sub", 0, 0, tiled=True)
    mine = arrived[:, :half_rows]
    parts = arrived[:, half_rows:].astype(jnp.float32).reshape(n_sub, 2 * tiles, out_rows, lanes)
    spread = parts[:, :tiles] + parts[:, tiles:]
    by_half = spread.reshape(n_sub // 2, 2, tiles, out_rows, lanes).sum(axis=0)
    projected = by_half.transpose(2, 0, 1, 3).reshape(out_rows, width)

    theirs = from_partner(mine, "sub", 1)
    picked_mine = jnp.take(mine, rows_all, axis=0)
    picked_theirs = jnp.take(theirs, rows_all, axis=0)
    picked_low = jnp.where(core == 0, picked_mine, picked_theirs)
    picked_high = jnp.where(core == 0, picked_theirs, picked_mine)
    picked = jnp.concatenate([picked_low, picked_high], axis=1)
    parent_sum = jnp.einsum("kab,kbm->am", vals_all, picked, preferred_element_type=jnp.float32)
    parent_out = parent_sum.astype(jnp.bfloat16)
    return (parent_out, projected)


def solution(mesh):
    return jax.shard_map(
        on_device,
        mesh=mesh,
        in_specs=(
            P(("group", "sub"), None),
            P(("group", "sub"), None, None),
            P(("group", "sub")),
            P(),
            P(("group", "sub"), None),
            P(("group", "sub"), None, None),
            P(("group", "sub")),
        ),
        out_specs=(P("sub", "group"), P(("group", "sub"), None)),
        check_vma=False,
    )
```

```python
import jax
import jax.numpy as jnp
from jax import lax
from jax.sharding import PartitionSpec as P

IFB = 8
BPR = 6


def from_partner(value, axis, mask):
    pairs = [(source, source ^ mask) for source in range(lax.axis_size(axis))]
    return lax.ppermute(value, axis, pairs)


def on_device(modes, block_vals, block_cols, level_maps, psi, parent_vals, parent_rows):
    block_size = block_vals.shape[1]
    width = modes.shape[1]
    vertex_blocks = modes.shape[0] // block_size
    row_blocks = IFB
    levels = min(2, lax.axis_size("group").bit_length() - 1)
    merged = 2**levels
    n_sub = lax.axis_size("sub")
    n_parent = parent_vals.shape[0]
    group_index = lax.axis_index("group")
    core = lax.axis_index("sub") % 2

    rows_as_block = jnp.zeros((16, block_size), jnp.bfloat16).at[0, :n_parent].set(parent_rows.astype(jnp.bfloat16))
    packed = jnp.concatenate([parent_vals.reshape(n_parent * block_size, block_size), rows_as_block], axis=0)

    onehot = (
        block_cols.reshape(row_blocks, BPR)[:, :, None] == jnp.arange(vertex_blocks)[None, None, :]
    ).astype(jnp.float32)
    blocks = block_vals.astype(jnp.float32).reshape(row_blocks, BPR, block_size, block_size)
    dense = (
        jnp.einsum("rbc,rbij->ricj", onehot, blocks)
        .reshape(row_blocks * block_size, vertex_blocks * block_size)
        .astype(jnp.bfloat16)
    )
    panel = jnp.dot(dense, modes, preferred_element_type=jnp.float32).astype(jnp.bfloat16)
    carried = packed[None]
    for level in range(levels):
        sibling = from_partner(panel, "group", 2**level)
        total = (panel.astype(jnp.float32) + sibling.astype(jnp.float32)).astype(jnp.bfloat16)
        if level == 0:
            carried, panel = lax.optimization_barrier((carried, panel))
            arrived = from_partner(carried, "group", 2**level)
            arrived, total = lax.optimization_barrier((arrived, total))
            carried = jnp.concatenate([carried, arrived], axis=0)
        mapped = jnp.einsum(
            "ab,rbm->ram",
            level_maps[level],
            total.reshape(row_blocks, block_size, width),
            preferred_element_type=jnp.float32,
        )
        panel = mapped.reshape(row_blocks * block_size, width).astype(jnp.bfloat16)
    quarter = width // merged
    half_rows = block_size // 2
    column = (group_index % merged) * quarter
    head = lax.dynamic_slice_in_dim(panel[:block_size], column, quarter, 1)

    half = width // 2
    keep_cols = lax.dynamic_slice_in_dim(panel, core * half, half, 1)
    send_cols = lax.dynamic_slice_in_dim(panel, (1 - core) * half, half, 1)
    contract = (((0,), (0,)), ((), ()))
    keep = lax.dot_general(psi, keep_cols, contract, preferred_element_type=jnp.float32)
    send = lax.dot_general(psi, send_cols, contract, preferred_element_type=jnp.float32)
    chip_sum = keep + from_partner(send, "sub", 1)
    lanes = 128
    tiles = half // lanes
    out_rows = width // n_sub
    col_tiles = [chip_sum[:, i * lanes : (i + 1) * lanes].reshape(n_sub, out_rows, lanes) for i in range(tiles)]
    highs = [lax.reduce_precision(t, exponent_bits=8, mantissa_bits=7) for t in col_tiles]
    lows = [t - h for t, h in zip(col_tiles, highs)]
    split = jnp.concatenate([h.astype(jnp.bfloat16) for h in highs] + [l.astype(jnp.bfloat16) for l in lows], axis=1)
    carried, head, split = lax.optimization_barrier((carried, head, split))
    carried = jnp.concatenate([carried, from_partner(carried, "group", 2 ** (levels - 1))], axis=0)
    vals_all = carried[:, : n_parent * block_size].reshape(-1, block_size, block_size)
    rows_all = carried[:, n_parent * block_size, :n_parent].reshape(-1).astype(jnp.int32)
    outgoing = jnp.tile(head.reshape(2, half_rows, quarter), (n_sub // 2, 1, 1))
    outgoing = jnp.concatenate([outgoing, split.reshape(n_sub, -1, quarter)], axis=1)
    arrived = lax.all_to_all(outgoing, "sub", 0, 0, tiled=True)
    mine = arrived[:, :half_rows]
    parts = arrived[:, half_rows:].astype(jnp.float32).reshape(n_sub, 2 * tiles, out_rows, lanes)
    spread = parts[:, :tiles] + parts[:, tiles:]
    by_half = spread.reshape(n_sub // 2, 2, tiles, out_rows, lanes).sum(axis=0)
    projected = by_half.transpose(2, 0, 1, 3).reshape(out_rows, width)

    theirs = from_partner(mine, "sub", 1)
    picked_mine = jnp.take(mine, rows_all, axis=0)
    picked_theirs = jnp.take(theirs, rows_all, axis=0)
    picked_low = jnp.where(core == 0, picked_mine, picked_theirs)
    picked_high = jnp.where(core == 0, picked_theirs, picked_mine)
    picked = jnp.concatenate([picked_low, picked_high], axis=1)
    parent_sum = jnp.einsum("kab,kbm->am", vals_all, picked, preferred_element_type=jnp.float32)
    parent_out = parent_sum.astype(jnp.bfloat16)
    return (parent_out, projected)


def solution(mesh):
    return jax.shard_map(
        on_device,
        mesh=mesh,
        in_specs=(
            P(("group", "sub"), None),
            P(("group", "sub"), None, None),
            P(("group", "sub")),
            P(),
            P(("group", "sub"), None),
            P(("group", "sub"), None, None),
            P(("group", "sub")),
        ),
        out_specs=(P("sub", "group"), P(("group", "sub"), None)),
        check_vma=False,
    )
```
